512 devices in a mesh: expert: 64 (over x, y, z_hi, core), dp: 8 (over z_lo).
Axes of the slice: x: 4, y: 4, z: 16 (z_hi: 2, z_lo: 8; z = z_hi * 8 + z_lo), core: 2. Of those that a mesh axis runs over, the one named last changes fastest.
Arguments:
- tokens: bfloat16 [256, 2048], P('dp'), may hold values from -6 to 6
- w_gate: bfloat16 [128, 768, 2048], P('expert', 'dp'), may hold values from -2 to 2
- w_up: bfloat16 [128, 768, 2048], P('expert', 'dp'), may hold values from -2 to 2
- w_down: bfloat16 [128, 768, 2048], P('expert', 'dp'), may hold values from -2 to 2
Outputs:
- cosine: float32 [256, 128, 128], P('expert')
The draws below stay inside these ranges and needn't reach their ends.
All inputs are finite; a program needn't handle non-finite values.
Results may differ from the reference program's by a relative error of at most 0.0014.
Values may be sent and summed in bfloat16 or wider, within the bound.
No kernel may reach another device: no remote copies, remote signals or barrier semaphores. Data moves between devices by JAX's collectives and lax.ppermute only.
A program may use at most 64 MiB of HBM per device.

```python
import jax
import jax.numpy as jnp
from jax import lax

D = 2048
H = 768
E = 128
TOKENS = 256


def expert_mix(key):
    return jax.random.uniform(jax.random.fold_in(key, 7), (E,), jnp.float32, 0.0, 0.95)


def mixed_weight(key, salt, shape, fan_in):
    common_key = jax.random.fold_in(key, salt)
    own_key = jax.random.fold_in(key, salt + 100)
    common = jax.random.normal(common_key, shape[1:], jnp.float32)
    own = jax.random.normal(own_key, shape, jnp.float32)
    mixing = expert_mix(key)[:, None, None]
    return (mixing * common[None] + jnp.sqrt(1.0 - mixing * mixing) * own) * fan_in ** (-0.5)


def draw_w_gate(key, part):
    return jnp.clip(mixed_weight(key, 11, (E, H, D), D), -2.0, 2.0).astype(jnp.bfloat16)


def draw_w_up(key, part):
    return jnp.clip(mixed_weight(key, 12, (E, H, D), D), -2.0, 2.0).astype(jnp.bfloat16)


def draw_w_down(key, part):
    column_scale = jnp.exp(jax.random.uniform(jax.random.fold_in(key, 313), (D,), jnp.float32, -1.15, 1.15))
    scaled = mixed_weight(key, 13, (E, H, D), H) * column_scale[None, None, :]
    return jnp.clip(scaled, -2.0, 2.0).astype(jnp.bfloat16)


def block_scale(stream_key, dims, cuts, low, high):
    def one(axis_at, blocks):
        heights = jax.random.uniform(jax.random.fold_in(jax.random.fold_in(stream_key, 6), axis_at), (blocks,), jnp.float32, low / len(cuts), high / len(cuts))
        return jnp.repeat(jnp.exp(heights), dims[axis_at] // blocks).reshape((-1,) + (1,) * (len(dims) - axis_at - 1))

    loudness = one(*cuts[0])
    for cut in cuts[1:]:
        loudness = loudness * one(*cut)
    return loudness


def bell_draw(key, extent, deviation, bound, cuts=(), held_as=jnp.bfloat16):
    factor_of = block_scale(key, extent, cuts, -0.22, 0.18) if cuts else 1.0
    array = jax.random.normal(key, extent, jnp.float32) * deviation * factor_of
    return jnp.minimum(jnp.maximum(array, -bound), bound).astype(held_as)


def setup_inputs(seed: int = 0) -> dict:
    streams_of = jax.random.split(jax.random.key(seed), 5)
    return {
        "tokens": bell_draw(streams_of[0], (TOKENS, D), 1.0, 6.0, ((0, 8),)),
        "w_gate": draw_w_gate(jax.random.fold_in(streams_of[4], 71), 0),
        "w_up": draw_w_up(jax.random.fold_in(streams_of[4], 71), 0),
        "w_down": draw_w_down(jax.random.fold_in(streams_of[4], 71), 0),
    }


def expert_outputs(tokens, gate_row, up_row, down_row):
    gate = jnp.dot(tokens, gate_row.T, preferred_element_type=jnp.float32)
    upward = jnp.dot(tokens, up_row.T, preferred_element_type=jnp.float32)
    hidden = (jax.nn.silu(gate) * upward).astype(jnp.bfloat16)
    total = jnp.dot(hidden, down_row, preferred_element_type=jnp.float32)
    return total.astype(jnp.bfloat16)

def reference(tokens, w_gate, w_up, w_down):
    outputs = lax.map(lambda weights: expert_outputs(tokens, weights[0], weights[1], weights[2]), (w_gate, w_up, w_down))
    wide = outputs.astype(jnp.float32)
    gram = jnp.einsum('etf,gtf->teg', wide, wide)
    diagonal = jnp.diagonal(gram, axis1=1, axis2=2)
    inverse = lax.rsqrt(diagonal + 1e-06)
    return gram * inverse[:, :, None] * inverse[:, None, :]
```

```python
import jax
import jax.numpy as jnp
from jax import lax
from jax.sharding import PartitionSpec as P


def all_reduce_dp(x, n):
    pieces = x.reshape((n, -1))
    mine = lax.all_to_all(pieces, "dp", 0, 0, tiled=True).sum(0, keepdims=True)
    spread = jnp.broadcast_to(mine, pieces.shape)
    return lax.all_to_all(spread, "dp", 0, 0, tiled=True).reshape(x.shape)


def shards(tokens, w_gate, w_up, w_down):
    n = lax.axis_size("dp")
    down_cols = lax.all_to_all(w_down, "dp", 2, 1, tiled=True)
    block_rows = lax.all_gather(tokens, "dp", axis=0, tiled=True)
    gate = jnp.einsum("td,ehd->eth", block_rows, w_gate, preferred_element_type=jnp.float32)
    upward = jnp.einsum("td,ehd->eth", block_rows, w_up, preferred_element_type=jnp.float32)
    hidden = (jax.nn.silu(gate) * upward).astype(jnp.bfloat16)
    hidden_all = lax.all_gather(hidden, "dp", axis=2, tiled=True)
    outputs = jnp.einsum("eth,ehf->etf", hidden_all, down_cols, preferred_element_type=jnp.float32)
    features = outputs.astype(jnp.bfloat16)
    regrouped = lax.all_to_all(features, "expert", 1, 0, tiled=True)
    partial_gram = jnp.einsum(
        "etf,gtf->teg", regrouped, regrouped, preferred_element_type=jnp.float32
    )
    gram = all_reduce_dp(partial_gram, n)
    diagonal = jnp.diagonal(gram, axis1=1, axis2=2)
    inverse = lax.rsqrt(diagonal + 1e-06)
    return gram * inverse[:, :, None] * inverse[:, None, :]


def solution(mesh):
    placed = (
        P("dp", None),
        P("expert", "dp", None),
        P("expert", "dp", None),
        P("expert", "dp", None),
    )
    return jax.shard_map(
        shards, mesh=mesh, in_specs=placed, out_specs=P("expert", None, None), check_vma=False
    )
```

```python
import jax
import jax.numpy as jnp
from jax import lax
from jax.sharding import PartitionSpec as P

BOTH = ("expert", "dp")


def z_ring_pairs(mesh, shift):
    axes = mesh.axis_names
    devs = mesh.devices.reshape(-1)
    index_of = {}
    for i, d in enumerate(devs):
        x, y, z = d.coords[:3]
        index_of[(x, y, z, d.core_on_chip)] = i
    z_len = 1 + max(k[2] for k in index_of)
    pairs = []
    for (x, y, z, c), i in index_of.items():
        pairs.append((i, index_of[(x, y, (z + shift) % z_len, c)]))
    assert axes == BOTH
    return sorted(pairs)


def gather_blocks(block, rings, n):
    k = lax.axis_index("dp")
    shifts = tuple(s for s, _ in rings)
    received = [block] + [lax.ppermute(block, BOTH, pairs) for _, pairs in rings]
    stacked = jnp.stack(received)
    source = (k - jnp.array((0,) + shifts)) % n
    ordered = jnp.take(stacked, jnp.argsort(source), axis=0)
    return ordered


def all_reduce_dp(x, n):
    pieces = x.reshape((n, -1))
    mine = lax.all_to_all(pieces, "dp", 0, 0, tiled=True).sum(0, keepdims=True)
    spread = jnp.broadcast_to(mine, pieces.shape)
    return lax.all_to_all(spread, "dp", 0, 0, tiled=True).reshape(x.shape)


def make_shards(mesh):
    n = mesh.shape["dp"]
    half = n // 2
    shifts = tuple(range(1, half + 1)) + tuple(-s for s in range(1, n - half))
    rings = tuple((s, z_ring_pairs(mesh, s)) for s in shifts)
    dp_shifts = tuple(range(1, n))

    def shards(tokens, w_gate, w_up, w_down):
        block_rows = gather_blocks(tokens, rings, n).reshape((-1, tokens.shape[1]))
        down_cols = lax.all_to_all(w_down, "dp", 2, 1, tiled=True)
        gate = jnp.einsum("td,ehd->eth", block_rows, w_gate, preferred_element_type=jnp.float32)
        upward = jnp.einsum("td,ehd->eth", block_rows, w_up, preferred_element_type=jnp.float32)
        hidden = (jax.nn.silu(gate) * upward).astype(jnp.bfloat16)
        k = lax.axis_index("dp")
        got = [hidden] + [
            lax.ppermute(hidden, "dp", [(i, (i + s) % n) for i in range(n)]) for s in dp_shifts
        ]
        stacked = jnp.stack(got)
        source = (k - jnp.arange(n)) % n
        hidden_all = jnp.take(stacked, jnp.argsort(source), axis=0)
        outputs = jnp.einsum(
            "keth,ekhf->etf",
            hidden_all,
            down_cols.reshape(w_down.shape[0], n, -1, down_cols.shape[2]),
            preferred_element_type=jnp.float32,
        )
        features = outputs.astype(jnp.bfloat16)
        regrouped = lax.all_to_all(features, "expert", 1, 0, tiled=True)
        partial_gram = jnp.einsum(
            "etf,gtf->teg", regrouped, regrouped, preferred_element_type=jnp.float32
        )
        gram = all_reduce_dp(partial_gram, n)
        eye = jnp.eye(gram.shape[1], dtype=jnp.bool_)
        diagonal = jnp.sum(jnp.where(eye[None], gram, 0.0), axis=2)
        inverse = lax.rsqrt(diagonal + 1e-06)
        return gram * inverse[:, :, None] * inverse[:, None, :]

    return shards


def solution(mesh):
    placed = (
        P("dp", None),
        P("expert", "dp", None),
        P("expert", "dp", None),
        P("expert", "dp", None),
    )
    return jax.shard_map(
        make_shards(mesh), mesh=mesh, in_specs=placed, out_specs=P("expert", None, None), check_vma=False
    )
```

```python
import jax
import jax.numpy as jnp
from jax import lax
from jax.sharding import PartitionSpec as P

BOTH = ("expert", "dp")


def z_ring_pairs(mesh, shift):
    axes = mesh.axis_names
    devs = mesh.devices.reshape(-1)
    index_of = {}
    for i, d in enumerate(devs):
        x, y, z = d.coords[:3]
        index_of[(x, y, z, d.core_on_chip)] = i
    z_len = 1 + max(k[2] for k in index_of)
    pairs = []
    for (x, y, z, c), i in index_of.items():
        pairs.append((i, index_of[(x, y, (z + shift) % z_len, c)]))
    assert axes == BOTH
    return sorted(pairs)


def gather_blocks(block, rings, n):
    k = lax.axis_index("dp")
    shifts = tuple(s for s, _ in rings)
    received = [block] + [lax.ppermute(block, BOTH, pairs) for _, pairs in rings]
    stacked = jnp.stack(received)
    source = (k - jnp.array((0,) + shifts)) % n
    ordered = jnp.take(stacked, jnp.argsort(source), axis=0)
    return ordered


def all_reduce_dp(x, n):
    pieces = x.reshape((n, -1))
    mine = lax.all_to_all(pieces, "dp", 0, 0, tiled=True).sum(0, keepdims=True)
    spread = jnp.broadcast_to(mine, pieces.shape)
    return lax.all_to_all(spread, "dp", 0, 0, tiled=True).reshape(x.shape)


def make_shards(mesh):
    n = mesh.shape["dp"]
    half = n // 2
    shifts = tuple(range(1, half + 1)) + tuple(-s for s in range(1, n - half))
    rings = tuple((s, z_ring_pairs(mesh, s)) for s in shifts)
    dp_shifts = tuple(range(1, n))

    def shards(tokens, w_gate, w_up, w_down):
        c = lax.axis_index("expert") % 2
        width = tokens.shape[1] // 2
        part = lax.dynamic_slice_in_dim(tokens, c * width, width, axis=1)
        mine = gather_blocks(part, rings, n).reshape((-1, width))
        other = lax.ppermute(mine, "expert", [(i, i ^ 1) for i in range(mesh.shape["expert"])])
        low = jnp.where(c == 0, mine, other)
        high = jnp.where(c == 0, other, mine)
        block_rows = jnp.concatenate([low, high], axis=1)
        down_cols = lax.all_to_all(w_down, "dp", 2, 1, tiled=True)
        gate = jnp.einsum("td,ehd->eth", block_rows, w_gate, preferred_element_type=jnp.float32)
        upward = jnp.einsum("td,ehd->eth", block_rows, w_up, preferred_element_type=jnp.float32)
        hidden = (jax.nn.silu(gate) * upward).astype(jnp.bfloat16)
        k = lax.axis_index("dp")
        got = [hidden] + [
            lax.ppermute(hidden, "dp", [(i, (i + s) % n) for i in range(n)]) for s in dp_shifts
        ]
        stacked = jnp.stack(got)
        source = (k - jnp.arange(n)) % n
        hidden_all = jnp.take(stacked, jnp.argsort(source), axis=0)
        outputs = jnp.einsum(
            "keth,ekhf->etf",
            hidden_all,
            down_cols.reshape(w_down.shape[0], n, -1, down_cols.shape[2]),
            preferred_element_type=jnp.float32,
        )
        features = outputs.astype(jnp.bfloat16)
        regrouped = lax.all_to_all(features, "expert", 1, 0, tiled=True)
        partial_gram = jnp.einsum(
            "etf,gtf->teg", regrouped, regrouped, preferred_element_type=jnp.float32
        )
        gram = all_reduce_dp(partial_gram, n)
        eye = jnp.eye(gram.shape[1], dtype=jnp.bool_)
        diagonal = jnp.sum(jnp.where(eye[None], gram, 0.0), axis=2)
        inverse = lax.rsqrt(diagonal + 1e-06)
        return gram * inverse[:, :, None] * inverse[:, None, :]

    return shards


def solution(mesh):
    placed = (
        P("dp", None),
        P("expert", "dp", None),
        P("expert", "dp", None),
        P("expert", "dp", None),
    )
    return jax.shard_map(
        make_shards(mesh), mesh=mesh, in_specs=placed, out_specs=P("expert", None, None), check_vma=False
    )
```

```python
import jax
import jax.numpy as jnp
from jax import lax
from jax.sharding import PartitionSpec as P

BOTH = ("expert", "dp")


def z_ring_pairs(mesh, shift):
    axes = mesh.axis_names
    devs = mesh.devices.reshape(-1)
    index_of = {}
    for i, d in enumerate(devs):
        x, y, z = d.coords[:3]
        index_of[(x, y, z, d.core_on_chip)] = i
    z_len = 1 + max(k[2] for k in index_of)
    pairs = []
    for (x, y, z, c), i in index_of.items():
        pairs.append((i, index_of[(x, y, (z + shift) % z_len, c)]))
    assert axes == BOTH
    return sorted(pairs)


def gather_blocks(block, rings, n):
    k = lax.axis_index("dp")
    shifts = tuple(s for s, _ in rings)
    received = [block] + [lax.ppermute(block, BOTH, pairs) for _, pairs in rings]
    stacked = jnp.stack(received)
    source = (k - jnp.array((0,) + shifts)) % n
    ordered = jnp.take(stacked, jnp.argsort(source), axis=0)
    return ordered


def doubling_gather(block, n):
    k = lax.axis_index("dp")
    have = block[None]
    codes = [0]
    step = n // 2
    while step:
        pairs = [(i, i ^ step) for i in range(n)]
        have = jnp.concatenate([have, lax.ppermute(have, "dp", pairs)], axis=0)
        codes = codes + [c ^ step for c in codes]
        step //= 2
    where = jnp.array(codes)
    position = jnp.argsort(where)
    return jnp.take(have, position[jnp.arange(n) ^ k], axis=0)


def all_reduce_dp(x, n):
    pieces = x.reshape((n, -1))
    mine = lax.all_to_all(pieces, "dp", 0, 0, tiled=True).sum(0, keepdims=True)
    spread = jnp.broadcast_to(mine, pieces.shape)
    return lax.all_to_all(spread, "dp", 0, 0, tiled=True).reshape(x.shape)


def make_shards(mesh):
    n = mesh.shape["dp"]
    half = n // 2
    shifts = tuple(range(1, half + 1)) + tuple(-s for s in range(1, n - half))
    rings = tuple((s, z_ring_pairs(mesh, s)) for s in shifts)
    dp_shifts = tuple(range(1, n))

    def shards(tokens, w_gate, w_up, w_down):
        c = lax.axis_index("expert") % 2
        width = tokens.shape[1] // 2
        part = lax.dynamic_slice_in_dim(tokens, c * width, width, axis=1)
        mine = gather_blocks(part, rings, n).reshape((-1, width))
        other = lax.ppermute(mine, "expert", [(i, i ^ 1) for i in range(mesh.shape["expert"])])
        low = jnp.where(c == 0, mine, other)
        high = jnp.where(c == 0, other, mine)
        block_rows = jnp.concatenate([low, high], axis=1)
        down_cols = lax.all_to_all(w_down, "dp", 2, 1, tiled=True)
        gate = jnp.einsum("td,ehd->eth", block_rows, w_gate, preferred_element_type=jnp.float32)
        upward = jnp.einsum("td,ehd->eth", block_rows, w_up, preferred_element_type=jnp.float32)
        hidden = (jax.nn.silu(gate) * upward).astype(jnp.bfloat16)
        hidden_all = doubling_gather(hidden, n)
        outputs = jnp.einsum(
            "keth,ekhf->etf",
            hidden_all,
            down_cols.reshape(w_down.shape[0], n, -1, down_cols.shape[2]),
            preferred_element_type=jnp.float32,
        )
        features = outputs.astype(jnp.bfloat16)
        regrouped = lax.all_to_all(features, "expert", 1, 0, tiled=True)
        partial_gram = jnp.einsum(
            "etf,gtf->teg", regrouped, regrouped, preferred_element_type=jnp.float32
        )
        gram = all_reduce_dp(partial_gram, n)
        eye = jnp.eye(gram.shape[1], dtype=jnp.bool_)
        diagonal = jnp.sum(jnp.where(eye[None], gram, 0.0), axis=2)
        inverse = lax.rsqrt(diagonal + 1e-06)
        return gram * inverse[:, :, None] * inverse[:, None, :]

    return shards


def solution(mesh):
    placed = (
        P("dp", None),
        P("expert", "dp", None),
        P("expert", "dp", None),
        P("expert", "dp", None),
    )
    return jax.shard_map(
        make_shards(mesh), mesh=mesh, in_specs=placed, out_specs=P("expert", None, None), check_vma=False
    )
```

```python
import jax
import jax.numpy as jnp
from jax import lax
from jax.sharding import PartitionSpec as P

BOTH = ("expert", "dp")


def z_ring_pairs(mesh, shift):
    axes = mesh.axis_names
    devs = mesh.devices.reshape(-1)
    index_of = {}
    for i, d in enumerate(devs):
        x, y, z = d.coords[:3]
        index_of[(x, y, z, d.core_on_chip)] = i
    z_len = 1 + max(k[2] for k in index_of)
    pairs = []
    for (x, y, z, c), i in index_of.items():
        pairs.append((i, index_of[(x, y, (z + shift) % z_len, c)]))
    assert axes == BOTH
    return sorted(pairs)


def gather_blocks(block, rings, n):
    k = lax.axis_index("dp")
    shifts = tuple(s for s, _ in rings)
    received = [block] + [lax.ppermute(block, BOTH, pairs) for _, pairs in rings]
    stacked = jnp.stack(received)
    source = (k - jnp.array((0,) + shifts)) % n
    ordered = jnp.take(stacked, jnp.argsort(source), axis=0)
    return ordered


def doubling_gather(block, n):
    k = lax.axis_index("dp")
    have = block[None]
    codes = [0]
    step = n // 2
    while step:
        pairs = [(i, i ^ step) for i in range(n)]
        have = jnp.concatenate([have, lax.ppermute(have, "dp", pairs)], axis=0)
        codes = codes + [c ^ step for c in codes]
        step //= 2
    where = jnp.array(codes)
    position = jnp.argsort(where)
    return jnp.take(have, position[jnp.arange(n) ^ k], axis=0)


def transpose_blocks(w, n):
    k = lax.axis_index("dp")
    width = w.shape[2] // n
    got = [lax.dynamic_slice_in_dim(w, k * width, width, axis=2)]
    for s in range(1, n):
        piece = lax.dynamic_slice_in_dim(w, ((k + s) % n) * width, width, axis=2)
        got.append(lax.ppermute(piece, "dp", [(i, (i + s) % n) for i in range(n)]))
    stacked = jnp.stack(got, axis=1)
    source = (k - jnp.arange(n)) % n
    ordered = jnp.take(stacked, jnp.argsort(source), axis=1)
    return ordered.reshape(w.shape[0], -1, width)


def all_reduce_dp(x, n):
    pieces = x.reshape((n, -1))
    mine = lax.all_to_all(pieces, "dp", 0, 0, tiled=True).sum(0, keepdims=True)
    spread = jnp.broadcast_to(mine, pieces.shape)
    return lax.all_to_all(spread, "dp", 0, 0, tiled=True).reshape(x.shape)


def make_shards(mesh):
    n = mesh.shape["dp"]
    half = n // 2
    shifts = tuple(range(1, half + 1)) + tuple(-s for s in range(1, n - half))
    rings = tuple((s, z_ring_pairs(mesh, s)) for s in shifts)
    dp_shifts = tuple(range(1, n))

    def shards(tokens, w_gate, w_up, w_down):
        c = lax.axis_index("expert") % 2
        width = tokens.shape[1] // 2
        part = lax.dynamic_slice_in_dim(tokens, c * width, width, axis=1)
        mine = gather_blocks(part, rings, n).reshape((-1, width))
        other = lax.ppermute(mine, "expert", [(i, i ^ 1) for i in range(mesh.shape["expert"])])
        low = jnp.where(c == 0, mine, other)
        high = jnp.where(c == 0, other, mine)
        block_rows = jnp.concatenate([low, high], axis=1)
        down_cols = transpose_blocks(w_down, n)
        gate = jnp.einsum("td,ehd->eth", block_rows, w_gate, preferred_element_type=jnp.float32)
        upward = jnp.einsum("td,ehd->eth", block_rows, w_up, preferred_element_type=jnp.float32)
        hidden = (jax.nn.silu(gate) * upward).astype(jnp.bfloat16)
        hidden_all = doubling_gather(hidden, n)
        outputs = jnp.einsum(
            "keth,ekhf->etf",
            hidden_all,
            down_cols.reshape(w_down.shape[0], n, -1, down_cols.shape[2]),
            preferred_element_type=jnp.float32,
        )
        features = outputs.astype(jnp.bfloat16)
        regrouped = lax.all_to_all(features, "expert", 1, 0, tiled=True)
        partial_gram = jnp.einsum(
            "etf,gtf->teg", regrouped, regrouped, preferred_element_type=jnp.float32
        )
        gram = all_reduce_dp(partial_gram, n)
        eye = jnp.eye(gram.shape[1], dtype=jnp.bool_)
        diagonal = jnp.sum(jnp.where(eye[None], gram, 0.0), axis=2)
        inverse = lax.rsqrt(diagonal + 1e-06)
        return gram * inverse[:, :, None] * inverse[:, None, :]

    return shards


def solution(mesh):
    placed = (
        P("dp", None),
        P("expert", "dp", None),
        P("expert", "dp", None),
        P("expert", "dp", None),
    )
    return jax.shard_map(
        make_shards(mesh), mesh=mesh, in_specs=placed, out_specs=P("expert", None, None), check_vma=False
    )
```

```python
import jax
import jax.numpy as jnp
from jax import lax
from jax.sharding import PartitionSpec as P

BOTH = ("expert", "dp")


def z_ring_pairs(mesh, shift):
    axes = mesh.axis_names
    devs = mesh.devices.reshape(-1)
    index_of = {}
    for i, d in enumerate(devs):
        x, y, z = d.coords[:3]
        index_of[(x, y, z, d.core_on_chip)] = i
    z_len = 1 + max(k[2] for k in index_of)
    pairs = []
    for (x, y, z, c), i in index_of.items():
        pairs.append((i, index_of[(x, y, (z + shift) % z_len, c)]))
    assert axes == BOTH
    return sorted(pairs)


def gather_blocks(block, rings, n):
    k = lax.axis_index("dp")
    shifts = tuple(s for s, _ in rings)
    received = [block] + [lax.ppermute(block, BOTH, pairs) for _, pairs in rings]
    stacked = jnp.stack(received)
    source = (k - jnp.array((0,) + shifts)) % n
    ordered = jnp.take(stacked, jnp.argsort(source), axis=0)
    return ordered


def doubling_gather(block, n):
    k = lax.axis_index("dp")
    have = block[None]
    codes = [0]
    step = n // 2
    while step:
        pairs = [(i, i ^ step) for i in range(n)]
        have = jnp.concatenate([have, lax.ppermute(have, "dp", pairs)], axis=0)
        codes = codes + [c ^ step for c in codes]
        step //= 2
    where = jnp.array(codes)
    position = jnp.argsort(where)
    return jnp.take(have, position[jnp.arange(n) ^ k], axis=0)


def transpose_blocks(w, n):
    k = lax.axis_index("dp")
    width = w.shape[2] // n
    got = [lax.dynamic_slice_in_dim(w, k * width, width, axis=2)]
    for s in range(1, n):
        piece = lax.dynamic_slice_in_dim(w, ((k + s) % n) * width, width, axis=2)
        got.append(lax.ppermute(piece, "dp", [(i, (i + s) % n) for i in range(n)]))
    stacked = jnp.stack(got, axis=1)
    source = (k - jnp.arange(n)) % n
    ordered = jnp.take(stacked, jnp.argsort(source), axis=1)
    return ordered.reshape(w.shape[0], -1, width)


def all_reduce_dp(x, n):
    pieces = x.reshape((n, -1))
    mine = lax.all_to_all(pieces, "dp", 0, 0, tiled=True).sum(0, keepdims=True)
    spread = jnp.broadcast_to(mine, pieces.shape)
    return lax.all_to_all(spread, "dp", 0, 0, tiled=True).reshape(x.shape)


def make_shards(mesh):
    n = mesh.shape["dp"]
    half = n // 2
    shifts = tuple(range(1, half + 1)) + tuple(-s for s in range(1, n - half))
    rings = tuple((s, z_ring_pairs(mesh, s)) for s in shifts)

    def body(tokens, w_gate, w_up, w_down):
        c = lax.axis_index("expert") % 2
        width = tokens.shape[1] // 2
        part = lax.dynamic_slice_in_dim(tokens, c * width, width, axis=1)
        mine = gather_blocks(part, rings, n).reshape((-1, width))
        other = lax.ppermute(mine, "expert", [(i, i ^ 1) for i in range(mesh.shape["expert"])])
        low = jnp.where(c == 0, mine, other)
        high = jnp.where(c == 0, other, mine)
        block_rows = jnp.concatenate([low, high], axis=1)
        down_cols = transpose_blocks(w_down, n)
        gate = jnp.einsum("td,ehd->eth", block_rows, w_gate, preferred_element_type=jnp.float32)
        upward = jnp.einsum("td,ehd->eth", block_rows, w_up, preferred_element_type=jnp.float32)
        hidden = (jax.nn.silu(gate) * upward).astype(jnp.bfloat16)
        hidden_all = doubling_gather(hidden, n)
        outputs = jnp.einsum(
            "keth,ekhf->etf",
            hidden_all,
            down_cols.reshape(w_down.shape[0], n, -1, down_cols.shape[2]),
            preferred_element_type=jnp.float32,
        )
        features = outputs.astype(jnp.bfloat16)
        regrouped = lax.all_to_all(features, "expert", 1, 0, tiled=True)
        partial_gram = jnp.einsum(
            "etf,gtf->teg", regrouped, regrouped, preferred_element_type=jnp.float32
        )
        gram = all_reduce_dp(partial_gram, n)
        eye = jnp.eye(gram.shape[1], dtype=jnp.bool_)
        diagonal = jnp.sum(jnp.where(eye[None], gram, 0.0), axis=2)
        inverse = lax.rsqrt(diagonal + 1e-06)
        return gram * inverse[:, :, None] * inverse[:, None, :]

    return body


def solution(mesh):
    placed = (
        P("dp", None),
        P("expert", "dp", None),
        P("expert", "dp", None),
        P("expert", "dp", None),
    )
    return jax.shard_map(
        make_shards(mesh), mesh=mesh, in_specs=placed, out_specs=P("expert", None, None), check_vma=False
    )
```

```python
import jax
import jax.numpy as jnp
from jax import lax
from jax.sharding import PartitionSpec as P

BOTH = ("expert", "dp")


def z_ring_pairs(mesh, shift):
    axes = mesh.axis_names
    devs = mesh.devices.reshape(-1)
    index_of = {}
    for i, d in enumerate(devs):
        x, y, z = d.coords[:3]
        index_of[(x, y, z, d.core_on_chip)] = i
    z_len = 1 + max(k[2] for k in index_of)
    pairs = []
    for (x, y, z, c), i in index_of.items():
        pairs.append((i, index_of[(x, y, (z + shift) % z_len, c)]))
    assert axes == BOTH
    return sorted(pairs)


def gather_blocks(block, rings, n):
    k = lax.axis_index("dp")
    shifts = tuple(s for s, _ in rings)
    received = [block] + [lax.ppermute(block, BOTH, pairs) for _, pairs in rings]
    stacked = jnp.stack(received)
    source = (k - jnp.array((0,) + shifts)) % n
    ordered = jnp.take(stacked, jnp.argsort(source), axis=0)
    return ordered


def doubling_gather(block, n):
    k = lax.axis_index("dp")
    have = block[None]
    codes = [0]
    step = n // 2
    while step:
        pairs = [(i, i ^ step) for i in range(n)]
        have = jnp.concatenate([have, lax.ppermute(have, "dp", pairs)], axis=0)
        codes = codes + [c ^ step for c in codes]
        step //= 2
    where = jnp.array(codes)
    position = jnp.argsort(where)
    return jnp.take(have, position[jnp.arange(n) ^ k], axis=0)


def transpose_blocks(w, n):
    k = lax.axis_index("dp")
    width = w.shape[2] // n
    got = [lax.dynamic_slice_in_dim(w, k * width, width, axis=2)]
    for s in range(1, n):
        piece = lax.dynamic_slice_in_dim(w, ((k + s) % n) * width, width, axis=2)
        got.append(lax.ppermute(piece, "dp", [(i, (i + s) % n) for i in range(n)]))
    stacked = jnp.stack(got, axis=1)
    source = (k - jnp.arange(n)) % n
    ordered = jnp.take(stacked, jnp.argsort(source), axis=1)
    return ordered.reshape(w.shape[0], -1, width)


def all_reduce_dp(x, n):
    pieces = x.reshape((n, -1))
    mine = lax.all_to_all(pieces, "dp", 0, 0, tiled=True).sum(0, keepdims=True)
    spread = jnp.broadcast_to(mine, pieces.shape)
    return lax.all_to_all(spread, "dp", 0, 0, tiled=True).reshape(x.shape)


def make_shards(mesh):
    n = mesh.shape["dp"]
    half = n // 2
    shifts = tuple(range(1, half + 1)) + tuple(-s for s in range(1, n - half))
    rings = tuple((s, z_ring_pairs(mesh, s)) for s in shifts)

    def body(tokens, w_gate, w_up, w_down):
        c = lax.axis_index("expert") % 2
        width = tokens.shape[1] // 2
        part = lax.dynamic_slice_in_dim(tokens, c * width, width, axis=1)
        mine = gather_blocks(part, rings, n).reshape((-1, width))
        other = lax.ppermute(mine, "expert", [(i, i ^ 1) for i in range(mesh.shape["expert"])])

        def half_dot(w):
            own_w = lax.dynamic_slice_in_dim(w, c * width, width, axis=2)
            other_w = lax.dynamic_slice_in_dim(w, (1 - c) * width, width, axis=2)
            first = jnp.einsum("td,ehd->eth", mine, own_w, preferred_element_type=jnp.float32)
            return first + jnp.einsum("td,ehd->eth", other, other_w, preferred_element_type=jnp.float32)

        down_cols = transpose_blocks(w_down, n)
        gate = half_dot(w_gate)
        upward = half_dot(w_up)
        hidden = (jax.nn.silu(gate) * upward).astype(jnp.bfloat16)
        hidden_all = doubling_gather(hidden, n)
        outputs = jnp.einsum(
            "keth,ekhf->etf",
            hidden_all,
            down_cols.reshape(w_down.shape[0], n, -1, down_cols.shape[2]),
            preferred_element_type=jnp.float32,
        )
        features = outputs.astype(jnp.bfloat16)
        regrouped = lax.all_to_all(features, "expert", 1, 0, tiled=True)
        partial_gram = jnp.einsum(
            "etf,gtf->teg", regrouped, regrouped, preferred_element_type=jnp.float32
        )
        gram = all_reduce_dp(partial_gram, n)
        eye = jnp.eye(gram.shape[1], dtype=jnp.bool_)
        diagonal = jnp.sum(jnp.where(eye[None], gram, 0.0), axis=2)
        inverse = lax.rsqrt(diagonal + 1e-06)
        return gram * inverse[:, :, None] * inverse[:, None, :]

    return body


def solution(mesh):
    placed = (
        P("dp", None),
        P("expert", "dp", None),
        P("expert", "dp", None),
        P("expert", "dp", None),
    )
    return jax.shard_map(
        make_shards(mesh), mesh=mesh, in_specs=placed, out_specs=P("expert", None, None), check_vma=False
    )
```
